512 devices in a mesh: ctx: 64 (over z, y_hi, core), chan: 8 (over x, y_lo).
Axes of the slice: x: 4, y: 4 (y_hi: 2, y_lo: 2; y = y_hi * 2 + y_lo), z: 16, core: 2. Of those that a mesh axis runs over, the one named last changes fastest.
Arguments:
- query_pol: bfloat16 [8192, 8192], P('chan', 'ctx'), may hold values from -6 to 6
- keys_pol: bfloat16 [8192, 8192], P('chan', 'ctx'), may hold values from -6 to 6
- value_pol: bfloat16 [8192, 8192], P('chan', 'ctx'), may hold values from -6 to 6
- filter_pol: float32 [4, 8192], P(None, 'ctx'), may hold values from -1.2 to 1.2
- skip_pol: float32 [8192], P('chan'), may hold values from -4 to 4
- query_ref: bfloat16 [8192, 8192], P('chan', 'ctx'), may hold values from -6 to 6
- keys_ref: bfloat16 [8192, 8192], P('chan', 'ctx'), may hold values from -6 to 6
- value_ref: bfloat16 [8192, 8192], P('chan', 'ctx'), may hold values from -6 to 6
- filter_ref: float32 [4, 8192], P(None, 'ctx'), may hold values from -1.2 to 1.2
- skip_ref: float32 [8192], P('chan'), may hold values from -4 to 4
- grad_out: bfloat16 [8192, 8192], P('chan', 'ctx'), may hold values from -0.75 to 0.75
Outputs:
- out_pol: bfloat16 [8192, 8192], P('chan', 'ctx')
- out_ref: bfloat16 [8192, 8192], P('chan', 'ctx')
- grad_query: bfloat16 [8192, 8192], P('chan', 'ctx')
- grad_keys: bfloat16 [8192, 8192], P('chan', 'ctx')
- grad_value: bfloat16 [8192, 8192], P('chan', 'ctx')
- grad_filter: float32 [4, 8192], P(None, 'ctx')
The draws below stay inside these ranges and needn't reach their ends.
All inputs are finite; a program needn't handle non-finite values.
Results may differ from the reference program's by a relative error of at most 0.003.
Values sent between devices are 32-bit elements; how exact they have to be, the bound alone decides.
No kernel may reach another device: no remote copies, remote signals or barrier semaphores. Data moves between devices by JAX's collectives and lax.ppermute only.
A program may use at most 64 MiB of HBM per device.

```python
import math
import jax
import jax.numpy as jnp

D = 8192
G = 4
L = 8192


def filter_draw(base_key, salt):
    mixed_key = jax.random.fold_in(base_key, salt)
    rate_key, noise_key = jax.random.split(mixed_key)
    lowest, highest = (0.3, L / 40.0)
    rates = jnp.exp(jax.random.uniform(rate_key, (G, 1), jnp.float32, math.log(lowest), math.log(highest)))
    positions = jnp.arange(L, dtype=jnp.float32)[None, :]
    noise = jax.random.truncated_normal(noise_key, -5.0, 5.0, (G, L), jnp.float32)
    return noise * jnp.sqrt(2.0 * rates / L) * jnp.exp(-rates * positions / L)


def draw_filter_pol(key, part):
    return filter_draw(key, 11)


def draw_filter_ref(key, part):
    return filter_draw(key, 23)


def block_levels(own_key, extent, cuts, low, high):
    factor_of = 1.0
    for position, shards_of in cuts:
        draws = jax.random.uniform(jax.random.fold_in(jax.random.fold_in(own_key, 6), position), (shards_of,), jnp.float32, low / len(cuts), high / len(cuts))
        factor_of = factor_of * jnp.repeat(jnp.exp(draws), extent[position] // shards_of).reshape((-1,) + (1,) * (len(extent) - 1 - position))
    return factor_of


def gaussian(rng, dims, width, reach, pieces=(), kind=jnp.bfloat16):
    entries = jax.random.normal(rng, dims, jnp.float32) * width
    if len(pieces) > 0:
        entries = block_levels(rng, dims, pieces, -0.22, 0.18) * entries
    return jnp.clip(entries, min=-reach, max=reach).astype(kind)


def setup_inputs(seed: int = 0) -> dict:
    arg_keys = jax.random.split(jax.random.key(seed), 12)
    return {
        "query_pol": gaussian(arg_keys[0], (D, L), 1.0, 6.0, ((0, 8), (1, 64))),
        "keys_pol": gaussian(arg_keys[1], (D, L), 1.0, 6.0, ((0, 8), (1, 64))),
        "value_pol": gaussian(arg_keys[2], (D, L), 1.0, 6.0, ((0, 8), (1, 64))),
        "filter_pol": draw_filter_pol(jax.random.fold_in(arg_keys[11], 71), 0),
        "skip_pol": gaussian(arg_keys[4], (D,), 1.0, 4.0, ((0, 8),), jnp.float32),
        "query_ref": gaussian(arg_keys[5], (D, L), 1.0, 6.0, ((0, 8), (1, 64))),
        "keys_ref": gaussian(arg_keys[6], (D, L), 1.0, 6.0, ((0, 8), (1, 64))),
        "value_ref": gaussian(arg_keys[7], (D, L), 1.0, 6.0, ((0, 8), (1, 64))),
        "filter_ref": draw_filter_ref(jax.random.fold_in(arg_keys[11], 71), 0),
        "skip_ref": gaussian(arg_keys[9], (D,), 1.0, 4.0, ((0, 8),), jnp.float32),
        "grad_out": gaussian(arg_keys[10], (D, L), 0.125, 0.75, ((0, 8), (1, 64))),
    }


def spectrum(fields, length):
    return jnp.fft.rfft(fields, n=2 * length, axis=-1)


def to_field(spec, length):
    return jnp.fft.irfft(spec, n=2 * length, axis=-1)[:, :length].astype(jnp.float32)


def reference(query_pol, keys_pol, value_pol, filter_pol, skip_pol, query_ref, keys_ref, value_ref, filter_ref, skip_ref, grad_out):
    length = query_pol.shape[1]
    gated_pol = keys_pol.astype(jnp.float32) * value_pol.astype(jnp.float32)
    gated_ref = keys_ref.astype(jnp.float32) * value_ref.astype(jnp.float32)
    filt_spec_pol = jnp.tile(spectrum(filter_pol, length), (D // G, 1))
    filt_spec_ref = jnp.tile(spectrum(filter_ref, length), (D // G, 1))
    gated_spec_pol = spectrum(gated_pol, length)
    gated_spec_ref = spectrum(gated_ref, length)
    mix_pol = to_field(gated_spec_pol * filt_spec_pol, length) + skip_pol[:, None] * gated_pol
    mix_ref = to_field(gated_spec_ref * filt_spec_ref, length) + skip_ref[:, None] * gated_ref
    out_pol = (query_pol.astype(jnp.float32) * mix_pol).astype(jnp.bfloat16)
    out_ref = (query_ref.astype(jnp.float32) * mix_ref).astype(jnp.bfloat16)
    out_grad = grad_out.astype(jnp.float32)
    grad_sum = out_grad * query_pol.astype(jnp.float32)
    grad_spec = spectrum(grad_sum, length)
    grad_mix = to_field(grad_spec * jnp.conj(filt_spec_pol), length) + skip_pol[:, None] * grad_sum
    grad_query = (out_grad * mix_pol).astype(jnp.bfloat16)
    grad_keys = (grad_mix * value_pol.astype(jnp.float32)).astype(jnp.bfloat16)
    grad_value = (grad_mix * keys_pol.astype(jnp.float32)).astype(jnp.bfloat16)
    cross = (grad_spec * jnp.conj(gated_spec_pol)).reshape(D // G, G, -1).sum(axis=0)
    grad_filter = to_field(cross, length)
    return out_pol, out_ref, grad_query, grad_keys, grad_value, grad_filter
```

```python
import jax
import jax.numpy as jnp
from jax import lax
from jax.sharding import PartitionSpec as P


def local(
    query_pol,
    keys_pol,
    value_pol,
    filter_pol,
    skip_pol,
    query_ref,
    keys_ref,
    value_ref,
    filter_ref,
    skip_ref,
    grad_out,
):
    chan_rows, span = query_pol.shape
    group_count = filter_pol.shape[0]
    gated_pol = keys_pol.astype(jnp.float32) * value_pol.astype(jnp.float32)
    gated_ref = keys_ref.astype(jnp.float32) * value_ref.astype(jnp.float32)
    out_grad = grad_out.astype(jnp.float32)
    grad_sum = out_grad * query_pol.astype(jnp.float32)

    stacked = jnp.stack([gated_pol, gated_ref, grad_sum])
    by_channel = lax.all_to_all(stacked, "ctx", split_axis=1, concat_axis=2, tiled=True)
    length = by_channel.shape[2]
    own_rows = by_channel.shape[1]
    filters = lax.all_gather(
        jnp.stack([filter_pol, filter_ref]), "ctx", axis=2, tiled=True
    )

    spec = jnp.fft.rfft(by_channel, n=2 * length, axis=-1)
    filt_spec = jnp.fft.rfft(filters, n=2 * length, axis=-1)
    grouped = spec.reshape(3, own_rows // group_count, group_count, -1)
    hpol = filt_spec[0][None]
    href = filt_spec[1][None]
    conv_pol = grouped[0] * hpol
    conv_ref = grouped[1] * href
    corr = grouped[2] * jnp.conj(hpol)
    cross = jnp.sum(grouped[2] * jnp.conj(grouped[0]), axis=0)
    prods = jnp.concatenate(
        [
            jnp.stack([conv_pol, conv_ref, corr]).reshape(3 * own_rows, -1),
            cross,
        ],
        axis=0,
    )
    fields = jnp.fft.irfft(prods, n=2 * length, axis=-1)[:, :length]
    back = fields[: 3 * own_rows].reshape(3, own_rows, length)
    partial_filter = fields[3 * own_rows :]

    returned = lax.all_to_all(back, "ctx", split_axis=2, concat_axis=1, tiled=True)
    grad_filter = lax.psum_scatter(partial_filter, "ctx", scatter_dimension=1, tiled=True)
    grad_filter = lax.psum(grad_filter, "chan")

    mix_pol = returned[0] + skip_pol[:, None] * gated_pol
    mix_ref = returned[1] + skip_ref[:, None] * gated_ref
    grad_mix = returned[2] + skip_pol[:, None] * grad_sum
    out_pol = (query_pol.astype(jnp.float32) * mix_pol).astype(jnp.bfloat16)
    out_ref = (query_ref.astype(jnp.float32) * mix_ref).astype(jnp.bfloat16)
    grad_query = (out_grad * mix_pol).astype(jnp.bfloat16)
    grad_keys = (grad_mix * value_pol.astype(jnp.float32)).astype(jnp.bfloat16)
    grad_value = (grad_mix * keys_pol.astype(jnp.float32)).astype(jnp.bfloat16)
    return (out_pol, out_ref, grad_query, grad_keys, grad_value, grad_filter)


def solution(mesh):
    in_specs = (
        P("chan", "ctx"),
        P("chan", "ctx"),
        P("chan", "ctx"),
        P(None, "ctx"),
        P("chan"),
        P("chan", "ctx"),
        P("chan", "ctx"),
        P("chan", "ctx"),
        P(None, "ctx"),
        P("chan"),
        P("chan", "ctx"),
    )
    out_specs = (
        P("chan", "ctx"),
        P("chan", "ctx"),
        P("chan", "ctx"),
        P("chan", "ctx"),
        P("chan", "ctx"),
        P(None, "ctx"),
    )
    return jax.shard_map(local, mesh=mesh, in_specs=in_specs, out_specs=out_specs, check_vma=False)
```

```python
import jax
import jax.numpy as jnp
from jax import lax
from jax.sharding import PartitionSpec as P


def local(
    query_pol,
    keys_pol,
    value_pol,
    filter_pol,
    skip_pol,
    query_ref,
    keys_ref,
    value_ref,
    filter_ref,
    skip_ref,
    grad_out,
):
    chan_rows, span = query_pol.shape
    group_count = filter_pol.shape[0]
    gated_pol = keys_pol.astype(jnp.float32) * value_pol.astype(jnp.float32)
    gated_ref = keys_ref.astype(jnp.float32) * value_ref.astype(jnp.float32)
    out_grad = grad_out.astype(jnp.float32)
    grad_sum = out_grad * query_pol.astype(jnp.float32)

    shards = lax.axis_size("ctx")
    own_rows = chan_rows // shards
    fields = jnp.stack([gated_pol, gated_ref, grad_sum])
    fields = fields.reshape(3, shards, own_rows, span).transpose(1, 0, 2, 3)
    fields = fields.reshape(shards, 3 * own_rows, span)
    filt = jnp.concatenate([filter_pol, filter_ref], axis=0)
    filt_rows = filt.shape[0]
    send = jnp.concatenate([fields, jnp.broadcast_to(filt[None], (shards, filt_rows, span))], axis=1)
    send = send.reshape(shards * (3 * own_rows + filt_rows), span)
    recv = lax.all_to_all(send, "ctx", split_axis=0, concat_axis=1, tiled=True)
    length = recv.shape[1]
    by_channel = recv[: 3 * own_rows].reshape(3, own_rows, length)
    filters = recv[3 * own_rows :].reshape(2, group_count, length)

    spec = jnp.fft.rfft(by_channel, n=2 * length, axis=-1)
    filt_spec = jnp.fft.rfft(filters, n=2 * length, axis=-1)
    grouped = spec.reshape(3, own_rows // group_count, group_count, -1)
    hpol = filt_spec[0][None]
    href = filt_spec[1][None]
    cross = jnp.sum(grouped[2] * jnp.conj(grouped[0]), axis=0)
    partial_filter = jnp.fft.irfft(cross, n=2 * length, axis=-1)[:, :length]
    partial_filter = lax.psum(partial_filter, "chan")
    conv_pol = grouped[0] * hpol
    conv_ref = grouped[1] * href
    corr = grouped[2] * jnp.conj(hpol)
    prods = jnp.stack([conv_pol, conv_ref, corr]).reshape(3 * own_rows, -1)
    fields_out = jnp.fft.irfft(prods, n=2 * length, axis=-1)[:, :length]
    back = jnp.concatenate([fields_out, partial_filter], axis=0)
    returned = lax.all_to_all(back, "ctx", split_axis=1, concat_axis=0, tiled=True)
    returned = returned.reshape(shards, 3 * own_rows + group_count, span)
    grad_filter = jnp.sum(returned[:, 3 * own_rows :], axis=0)
    returned = returned[:, : 3 * own_rows].reshape(shards, 3, own_rows, span)
    returned = returned.transpose(1, 0, 2, 3).reshape(3, chan_rows, span)

    mix_pol = returned[0] + skip_pol[:, None] * gated_pol
    mix_ref = returned[1] + skip_ref[:, None] * gated_ref
    grad_mix = returned[2] + skip_pol[:, None] * grad_sum
    out_pol = (query_pol.astype(jnp.float32) * mix_pol).astype(jnp.bfloat16)
    out_ref = (query_ref.astype(jnp.float32) * mix_ref).astype(jnp.bfloat16)
    grad_query = (out_grad * mix_pol).astype(jnp.bfloat16)
    grad_keys = (grad_mix * value_pol.astype(jnp.float32)).astype(jnp.bfloat16)
    grad_value = (grad_mix * keys_pol.astype(jnp.float32)).astype(jnp.bfloat16)
    return (out_pol, out_ref, grad_query, grad_keys, grad_value, grad_filter)


def solution(mesh):
    in_specs = (
        P("chan", "ctx"),
        P("chan", "ctx"),
        P("chan", "ctx"),
        P(None, "ctx"),
        P("chan"),
        P("chan", "ctx"),
        P("chan", "ctx"),
        P("chan", "ctx"),
        P(None, "ctx"),
        P("chan"),
        P("chan", "ctx"),
    )
    out_specs = (
        P("chan", "ctx"),
        P("chan", "ctx"),
        P("chan", "ctx"),
        P("chan", "ctx"),
        P("chan", "ctx"),
        P(None, "ctx"),
    )
    return jax.shard_map(local, mesh=mesh, in_specs=in_specs, out_specs=out_specs, check_vma=False)
```

```python
import math

import jax
import jax.numpy as jnp
import numpy as np
from jax import lax
from jax.sharding import PartitionSpec as P

PREC = lax.Precision.HIGH
LANES = 128


def dft_tables(length):
    full = 2 * length
    width = LANES
    outer = full // width
    used = length // width
    a = np.arange(outer)
    b = np.arange(width)
    turn_a = 2.0 * math.pi * ((a[:, None] * a[None, :]) % outer) / outer
    turn_t = 2.0 * math.pi * ((a[:, None] * b[None, :]) % full) / full
    turn_b = 2.0 * math.pi * ((b[:, None] * b[None, :]) % width) / width
    ca, sa = np.cos(turn_a), np.sin(turn_a)
    ct, st = np.cos(turn_t), np.sin(turn_t)
    cb, sb = np.cos(turn_b), np.sin(turn_b)
    fwd_a = np.stack([ca[:, :used], -sa[:, :used]])
    fwd_b = np.block([[cb, -sb], [sb, cb]])
    inv_b = np.block([[cb, sb], [-sb, cb]])
    inv_a = np.stack([ca[:, :used], -sa[:, :used]]) / full
    f32 = lambda t: jnp.asarray(t.astype(np.float32))
    return dict(
        fwd_a=f32(fwd_a), fwd_b=f32(fwd_b), inv_b=f32(inv_b), inv_a=f32(inv_a),
        ct=f32(ct), st=f32(st), outer=outer, used=used, width=width,
    )


def forward_dft(x, tab):
    rows = x.shape[0]
    xa = x.reshape(rows, tab["used"], tab["width"])
    y = jnp.einsum("rab,cka->rckb", xa, tab["fwd_a"], precision=PREC)
    yr, yi = y[:, 0], y[:, 1]
    ct, st = tab["ct"], tab["st"]
    zr = yr * ct + yi * st
    zi = yi * ct - yr * st
    z = jnp.concatenate([zr, zi], axis=-1)
    return jnp.einsum("rkb,bm->rkm", z, tab["fwd_b"], precision=PREC)


def inverse_dft(p, tab):
    rows = p.shape[0]
    width = tab["width"]
    q = jnp.einsum("rkb,bm->rkm", p, tab["inv_b"], precision=PREC)
    qr, qi = q[..., :width], q[..., width:]
    ct, st = tab["ct"], tab["st"]
    q2 = jnp.stack([qr * ct - qi * st, qr * st + qi * ct], axis=1)
    y = jnp.einsum("rckb,cka->rab", q2, tab["inv_a"], precision=PREC)
    return y.reshape(rows, tab["used"] * width)


def cmul(x, h, conj_h, width):
    xr, xi = x[..., :width], x[..., width:]
    hr, hi = h[..., :width], h[..., width:]
    if conj_h:
        return jnp.concatenate([xr * hr + xi * hi, xi * hr - xr * hi], axis=-1)
    return jnp.concatenate([xr * hr - xi * hi, xr * hi + xi * hr], axis=-1)


def local(
    query_pol,
    keys_pol,
    value_pol,
    filter_pol,
    skip_pol,
    query_ref,
    keys_ref,
    value_ref,
    filter_ref,
    skip_ref,
    grad_out,
):
    chan_rows, span = query_pol.shape
    group_count = filter_pol.shape[0]
    gated_pol = keys_pol.astype(jnp.float32) * value_pol.astype(jnp.float32)
    gated_ref = keys_ref.astype(jnp.float32) * value_ref.astype(jnp.float32)
    out_grad = grad_out.astype(jnp.float32)
    grad_sum = out_grad * query_pol.astype(jnp.float32)

    shards = lax.axis_size("ctx")
    own_rows = chan_rows // shards
    fields = jnp.stack([gated_pol, gated_ref, grad_sum])
    fields = fields.reshape(3, shards, own_rows, span).transpose(1, 0, 2, 3)
    fields = fields.reshape(shards, 3 * own_rows, span)
    filt = jnp.concatenate([filter_pol, filter_ref], axis=0)
    filt_rows = filt.shape[0]
    send = jnp.concatenate([fields, jnp.broadcast_to(filt[None], (shards, filt_rows, span))], axis=1)
    send = send.reshape(shards * (3 * own_rows + filt_rows), span)
    recv = lax.all_to_all(send, "ctx", split_axis=0, concat_axis=1, tiled=True)
    length = recv.shape[1]
    tab = dft_tables(length)
    width = tab["width"]

    spec = forward_dft(recv, tab)
    outer = spec.shape[1]
    fspec = spec[: 3 * own_rows].reshape(3, own_rows // group_count, group_count, outer, 2 * width)
    hspec = spec[3 * own_rows :].reshape(2, 1, group_count, outer, 2 * width)
    conv_pol = cmul(fspec[0], hspec[0], False, width)
    conv_ref = cmul(fspec[1], hspec[1], False, width)
    corr = cmul(fspec[2], hspec[0], True, width)
    cross = jnp.sum(cmul(fspec[2], fspec[0], True, width), axis=0)
    prods = jnp.concatenate(
        [
            jnp.stack([conv_pol, conv_ref, corr]).reshape(3 * own_rows, outer, 2 * width),
            cross,
        ],
        axis=0,
    )
    back = inverse_dft(prods, tab)
    returned = lax.all_to_all(back, "ctx", split_axis=1, concat_axis=0, tiled=True)
    returned = returned.reshape(shards, 3 * own_rows + group_count, span)
    grad_filter = jnp.sum(returned[:, 3 * own_rows :], axis=0)
    grad_filter = lax.psum(grad_filter, "chan")
    returned = returned[:, : 3 * own_rows].reshape(shards, 3, own_rows, span)
    returned = returned.transpose(1, 0, 2, 3).reshape(3, chan_rows, span)

    mix_pol = returned[0] + skip_pol[:, None] * gated_pol
    mix_ref = returned[1] + skip_ref[:, None] * gated_ref
    grad_mix = returned[2] + skip_pol[:, None] * grad_sum
    out_pol = (query_pol.astype(jnp.float32) * mix_pol).astype(jnp.bfloat16)
    out_ref = (query_ref.astype(jnp.float32) * mix_ref).astype(jnp.bfloat16)
    grad_query = (out_grad * mix_pol).astype(jnp.bfloat16)
    grad_keys = (grad_mix * value_pol.astype(jnp.float32)).astype(jnp.bfloat16)
    grad_value = (grad_mix * keys_pol.astype(jnp.float32)).astype(jnp.bfloat16)
    return (out_pol, out_ref, grad_query, grad_keys, grad_value, grad_filter)


def solution(mesh):
    in_specs = (
        P("chan", "ctx"),
        P("chan", "ctx"),
        P("chan", "ctx"),
        P(None, "ctx"),
        P("chan"),
        P("chan", "ctx"),
        P("chan", "ctx"),
        P("chan", "ctx"),
        P(None, "ctx"),
        P("chan"),
        P("chan", "ctx"),
    )
    out_specs = (
        P("chan", "ctx"),
        P("chan", "ctx"),
        P("chan", "ctx"),
        P("chan", "ctx"),
        P("chan", "ctx"),
        P(None, "ctx"),
    )
    return jax.shard_map(local, mesh=mesh, in_specs=in_specs, out_specs=out_specs, check_vma=False)
```

```python
import math

import jax
import jax.numpy as jnp
import numpy as np
from jax import lax
from jax.sharding import PartitionSpec as P

PREC = lax.Precision.HIGH
LANES = 128


def dft_tables(length):
    full = 2 * length
    width = LANES
    outer = full // width
    used = length // width
    a = np.arange(outer)
    b = np.arange(width)
    turn_a = 2.0 * math.pi * ((a[:, None] * a[None, :]) % outer) / outer
    turn_t = 2.0 * math.pi * ((a[:, None] * b[None, :]) % full) / full
    turn_b = 2.0 * math.pi * ((b[:, None] * b[None, :]) % width) / width
    ca, sa = np.cos(turn_a), np.sin(turn_a)
    ct, st = np.cos(turn_t), np.sin(turn_t)
    cb, sb = np.cos(turn_b), np.sin(turn_b)
    fwd_a = np.stack([ca[:, :used], -sa[:, :used]])
    fwd_b = np.block([[cb, -sb], [sb, cb]])
    inv_b = np.block([[cb, sb], [-sb, cb]])
    inv_a = np.stack([ca[:, :used], -sa[:, :used]]) / full
    f32 = lambda t: jnp.asarray(t.astype(np.float32))
    return dict(
        fwd_a=f32(fwd_a), fwd_b=f32(fwd_b), inv_b=f32(inv_b), inv_a=f32(inv_a),
        ct=f32(ct), st=f32(st), outer=outer, used=used, width=width,
    )


def forward_dft(x, tab):
    rows = x.shape[0]
    xa = x.reshape(rows, tab["used"], tab["width"])
    y = jnp.einsum("rab,cka->rckb", xa, tab["fwd_a"], precision=PREC)
    yr, yi = y[:, 0], y[:, 1]
    ct, st = tab["ct"], tab["st"]
    zr = yr * ct + yi * st
    zi = yi * ct - yr * st
    z = jnp.concatenate([zr, zi], axis=-1)
    return jnp.einsum("rkb,bm->rkm", z, tab["fwd_b"], precision=PREC)


def inverse_dft(p, tab):
    rows = p.shape[0]
    width = tab["width"]
    q = jnp.einsum("rkb,bm->rkm", p, tab["inv_b"], precision=PREC)
    qr, qi = q[..., :width], q[..., width:]
    ct, st = tab["ct"], tab["st"]
    q2 = jnp.stack([qr * ct - qi * st, qr * st + qi * ct], axis=1)
    y = jnp.einsum("rckb,cka->rab", q2, tab["inv_a"], precision=PREC)
    return y.reshape(rows, tab["used"] * width)


def cmul(x, h, conj_h, width):
    xr, xi = x[..., :width], x[..., width:]
    hr, hi = h[..., :width], h[..., width:]
    if conj_h:
        return jnp.concatenate([xr * hr + xi * hi, xi * hr - xr * hi], axis=-1)
    return jnp.concatenate([xr * hr - xi * hi, xr * hi + xi * hr], axis=-1)


def local(
    query_pol,
    keys_pol,
    value_pol,
    filter_pol,
    skip_pol,
    query_ref,
    keys_ref,
    value_ref,
    filter_ref,
    skip_ref,
    grad_out,
):
    chan_rows, span = query_pol.shape
    group_count = filter_pol.shape[0]
    gated_pol = keys_pol.astype(jnp.float32) * value_pol.astype(jnp.float32)
    gated_ref = keys_ref.astype(jnp.float32) * value_ref.astype(jnp.float32)
    out_grad = grad_out.astype(jnp.float32)
    grad_sum = out_grad * query_pol.astype(jnp.float32)

    shards = lax.axis_size("ctx")
    own_rows = chan_rows // shards

    def to_channels(parts, extra):
        count = len(parts)
        block = jnp.stack(parts).reshape(count, shards, own_rows, span).transpose(1, 0, 2, 3)
        block = block.reshape(shards, count * own_rows, span)
        if extra is not None:
            block = jnp.concatenate(
                [block, jnp.broadcast_to(extra[None], (shards,) + extra.shape)], axis=1
            )
        block = block.reshape(-1, span)
        return lax.all_to_all(block, "ctx", split_axis=0, concat_axis=1, tiled=True)

    def to_positions(block, count):
        got = lax.all_to_all(block, "ctx", split_axis=1, concat_axis=0, tiled=True)
        got = got.reshape(shards, -1, span)
        fields_back = got[:, : count * own_rows].reshape(shards, count, own_rows, span)
        fields_back = fields_back.transpose(1, 0, 2, 3).reshape(count, chan_rows, span)
        return fields_back, got[:, count * own_rows :]

    filt = jnp.concatenate([filter_pol, filter_ref], axis=0)
    recv_pol = to_channels([gated_pol, grad_sum], filt)
    recv_ref = to_channels([gated_ref], None)
    length = recv_pol.shape[1]
    tab = dft_tables(length)
    width = tab["width"]
    groups_per = own_rows // group_count

    spec = forward_dft(recv_pol, tab)
    outer = spec.shape[1]
    fspec = spec[: 2 * own_rows].reshape(2, groups_per, group_count, outer, 2 * width)
    hspec = spec[2 * own_rows :].reshape(2, 1, group_count, outer, 2 * width)
    conv_pol = cmul(fspec[0], hspec[0], False, width)
    corr = cmul(fspec[1], hspec[0], True, width)
    cross = jnp.sum(cmul(fspec[1], fspec[0], True, width), axis=0)
    prods = jnp.concatenate(
        [jnp.stack([conv_pol, corr]).reshape(2 * own_rows, outer, 2 * width), cross], axis=0
    )
    pol_back, partial = to_positions(inverse_dft(prods, tab), 2)

    spec_ref = forward_dft(recv_ref, tab).reshape(groups_per, group_count, outer, 2 * width)
    conv_ref = cmul(spec_ref, hspec[1], False, width).reshape(own_rows, outer, 2 * width)
    ref_back, _ = to_positions(inverse_dft(conv_ref, tab), 1)

    grad_filter = lax.psum(jnp.sum(partial, axis=0), "chan")
    returned = (pol_back[0], ref_back[0], pol_back[1])

    mix_pol = returned[0] + skip_pol[:, None] * gated_pol
    mix_ref = returned[1] + skip_ref[:, None] * gated_ref
    grad_mix = returned[2] + skip_pol[:, None] * grad_sum
    out_pol = (query_pol.astype(jnp.float32) * mix_pol).astype(jnp.bfloat16)
    out_ref = (query_ref.astype(jnp.float32) * mix_ref).astype(jnp.bfloat16)
    grad_query = (out_grad * mix_pol).astype(jnp.bfloat16)
    grad_keys = (grad_mix * value_pol.astype(jnp.float32)).astype(jnp.bfloat16)
    grad_value = (grad_mix * keys_pol.astype(jnp.float32)).astype(jnp.bfloat16)
    return (out_pol, out_ref, grad_query, grad_keys, grad_value, grad_filter)


def solution(mesh):
    in_specs = (
        P("chan", "ctx"),
        P("chan", "ctx"),
        P("chan", "ctx"),
        P(None, "ctx"),
        P("chan"),
        P("chan", "ctx"),
        P("chan", "ctx"),
        P("chan", "ctx"),
        P(None, "ctx"),
        P("chan"),
        P("chan", "ctx"),
    )
    out_specs = (
        P("chan", "ctx"),
        P("chan", "ctx"),
        P("chan", "ctx"),
        P("chan", "ctx"),
        P("chan", "ctx"),
        P(None, "ctx"),
    )
    return jax.shard_map(local, mesh=mesh, in_specs=in_specs, out_specs=out_specs, check_vma=False)
```

```python
import math

import jax
import jax.numpy as jnp
import numpy as np
from jax import lax
from jax.sharding import PartitionSpec as P

PREC = lax.Precision.HIGH
LANES = 128


def dft_tables(length):
    full = 2 * length
    width = LANES
    outer = full // width
    used = length // width
    a = np.arange(outer)
    b = np.arange(width)
    turn_a = 2.0 * math.pi * ((a[:, None] * a[None, :]) % outer) / outer
    turn_t = 2.0 * math.pi * ((a[:, None] * b[None, :]) % full) / full
    turn_b = 2.0 * math.pi * ((b[:, None] * b[None, :]) % width) / width
    ca, sa = np.cos(turn_a), np.sin(turn_a)
    ct, st = np.cos(turn_t), np.sin(turn_t)
    cb, sb = np.cos(turn_b), np.sin(turn_b)
    fwd_a = np.stack([ca[:, :used], -sa[:, :used]])
    fwd_b = np.block([[cb, -sb], [sb, cb]])
    inv_b = np.block([[cb, sb], [-sb, cb]])
    inv_a = np.stack([ca[:, :used], -sa[:, :used]]) / full
    f32 = lambda t: jnp.asarray(t.astype(np.float32))
    return dict(
        fwd_a=f32(fwd_a), fwd_b=f32(fwd_b), inv_b=f32(inv_b), inv_a=f32(inv_a),
        ct=f32(ct), st=f32(st), outer=outer, used=used, width=width,
    )


def forward_dft(x, tab):
    rows = x.shape[0]
    xa = x.reshape(rows, tab["used"], tab["width"])
    y = jnp.einsum("rab,cka->rckb", xa, tab["fwd_a"], precision=PREC)
    yr, yi = y[:, 0], y[:, 1]
    ct, st = tab["ct"], tab["st"]
    zr = yr * ct + yi * st
    zi = yi * ct - yr * st
    z = jnp.concatenate([zr, zi], axis=-1)
    return jnp.einsum("rkb,bm->rkm", z, tab["fwd_b"], precision=PREC)


def inverse_dft(p, tab):
    rows = p.shape[0]
    width = tab["width"]
    q = jnp.einsum("rkb,bm->rkm", p, tab["inv_b"], precision=PREC)
    qr, qi = q[..., :width], q[..., width:]
    ct, st = tab["ct"], tab["st"]
    q2 = jnp.stack([qr * ct - qi * st, qr * st + qi * ct], axis=1)
    y = jnp.einsum("rckb,cka->rab", q2, tab["inv_a"], precision=PREC)
    return y.reshape(rows, tab["used"] * width)


def cmul(x, h, conj_h, width):
    xr, xi = x[..., :width], x[..., width:]
    hr, hi = h[..., :width], h[..., width:]
    if conj_h:
        return jnp.concatenate([xr * hr + xi * hi, xi * hr - xr * hi], axis=-1)
    return jnp.concatenate([xr * hr - xi * hi, xr * hi + xi * hr], axis=-1)


def local(
    query_pol,
    keys_pol,
    value_pol,
    filter_pol,
    skip_pol,
    query_ref,
    keys_ref,
    value_ref,
    filter_ref,
    skip_ref,
    grad_out,
):
    chan_rows, span = query_pol.shape
    group_count = filter_pol.shape[0]
    gated_pol = keys_pol.astype(jnp.float32) * value_pol.astype(jnp.float32)
    gated_ref = keys_ref.astype(jnp.float32) * value_ref.astype(jnp.float32)
    out_grad = grad_out.astype(jnp.float32)
    grad_sum = out_grad * query_pol.astype(jnp.float32)

    shards = lax.axis_size("ctx")
    own_rows = chan_rows // shards
    blocks = shards // group_count
    fields = jnp.stack([gated_pol, gated_ref, grad_sum])
    fields = fields.reshape(3, blocks, own_rows, group_count, span).transpose(1, 3, 0, 2, 4)
    fields = fields.reshape(shards, 3 * own_rows, span)
    filt = jnp.stack([filter_pol, filter_ref], axis=1)
    filt_rows = filt.shape[1]
    filt = jnp.broadcast_to(filt[None], (blocks, group_count, filt_rows, span))
    send = jnp.concatenate([fields, filt.reshape(shards, filt_rows, span)], axis=1)
    send = send.reshape(shards * (3 * own_rows + filt_rows), span)
    recv = lax.all_to_all(send, "ctx", split_axis=0, concat_axis=1, tiled=True)
    length = recv.shape[1]
    tab = dft_tables(length)
    width = tab["width"]

    spec = forward_dft(recv, tab)
    outer = spec.shape[1]
    fspec = spec[: 3 * own_rows].reshape(3, own_rows, outer, 2 * width)
    hpol = spec[3 * own_rows : 3 * own_rows + 1]
    href = spec[3 * own_rows + 1 :]
    conv_pol = cmul(fspec[0], hpol, False, width)
    conv_ref = cmul(fspec[1], href, False, width)
    corr = cmul(fspec[2], hpol, True, width)
    cross = jnp.sum(cmul(fspec[2], fspec[0], True, width), axis=0, keepdims=True)
    prods = jnp.concatenate([conv_pol, conv_ref, corr, cross], axis=0)
    back = inverse_dft(prods, tab)
    returned = lax.all_to_all(back, "ctx", split_axis=1, concat_axis=0, tiled=True)
    returned = returned.reshape(blocks, group_count, 3 * own_rows + 1, span)
    grad_filter = jnp.sum(returned[:, :, 3 * own_rows], axis=0)
    grad_filter = lax.psum(grad_filter, "chan")
    returned = returned[:, :, : 3 * own_rows].reshape(blocks, group_count, 3, own_rows, span)
    returned = returned.transpose(2, 0, 3, 1, 4).reshape(3, chan_rows, span)

    mix_pol = returned[0] + skip_pol[:, None] * gated_pol
    mix_ref = returned[1] + skip_ref[:, None] * gated_ref
    grad_mix = returned[2] + skip_pol[:, None] * grad_sum
    out_pol = (query_pol.astype(jnp.float32) * mix_pol).astype(jnp.bfloat16)
    out_ref = (query_ref.astype(jnp.float32) * mix_ref).astype(jnp.bfloat16)
    grad_query = (out_grad * mix_pol).astype(jnp.bfloat16)
    grad_keys = (grad_mix * value_pol.astype(jnp.float32)).astype(jnp.bfloat16)
    grad_value = (grad_mix * keys_pol.astype(jnp.float32)).astype(jnp.bfloat16)
    return (out_pol, out_ref, grad_query, grad_keys, grad_value, grad_filter)


def solution(mesh):
    in_specs = (
        P("chan", "ctx"),
        P("chan", "ctx"),
        P("chan", "ctx"),
        P(None, "ctx"),
        P("chan"),
        P("chan", "ctx"),
        P("chan", "ctx"),
        P("chan", "ctx"),
        P(None, "ctx"),
        P("chan"),
        P("chan", "ctx"),
    )
    out_specs = (
        P("chan", "ctx"),
        P("chan", "ctx"),
        P("chan", "ctx"),
        P("chan", "ctx"),
        P("chan", "ctx"),
        P(None, "ctx"),
    )
    return jax.shard_map(local, mesh=mesh, in_specs=in_specs, out_specs=out_specs, check_vma=False)
```

```python
import math

import jax
import jax.numpy as jnp
import numpy as np
from jax import lax
from jax.sharding import PartitionSpec as P

PREC = lax.Precision.HIGH
LANES = 128


def dft_tables(length):
    full = 2 * length
    width = LANES
    outer = full // width
    used = length // width
    a = np.arange(outer)
    b = np.arange(width)
    turn_a = 2.0 * math.pi * ((a[:, None] * a[None, :]) % outer) / outer
    turn_t = 2.0 * math.pi * ((a[:, None] * b[None, :]) % full) / full
    turn_b = 2.0 * math.pi * ((b[:, None] * b[None, :]) % width) / width
    ca, sa = np.cos(turn_a), np.sin(turn_a)
    ct, st = np.cos(turn_t), np.sin(turn_t)
    cb, sb = np.cos(turn_b), np.sin(turn_b)
    fwd_a = np.stack([ca[:, :used], -sa[:, :used]])
    fwd_b = np.block([[cb, -sb], [sb, cb]])
    inv_b = np.block([[cb, sb], [-sb, cb]])
    inv_a = np.stack([ca[:, :used], -sa[:, :used]]) / full
    f32 = lambda t: jnp.asarray(t.astype(np.float32))
    return dict(
        fwd_a=f32(fwd_a), fwd_b=f32(fwd_b), inv_b=f32(inv_b), inv_a=f32(inv_a),
        ct=f32(ct), st=f32(st), outer=outer, used=used, width=width,
    )


def forward_dft(x, tab):
    rows = x.shape[0]
    xa = x.reshape(rows, tab["used"], tab["width"])
    y = jnp.einsum("rab,cka->rckb", xa, tab["fwd_a"], precision=PREC)
    yr, yi = y[:, 0], y[:, 1]
    ct, st = tab["ct"], tab["st"]
    zr = yr * ct + yi * st
    zi = yi * ct - yr * st
    z = jnp.concatenate([zr, zi], axis=-1)
    return jnp.einsum("rkb,bm->rkm", z, tab["fwd_b"], precision=PREC)


def inverse_dft(p, tab):
    rows = p.shape[0]
    width = tab["width"]
    q = jnp.einsum("rkb,bm->rkm", p, tab["inv_b"], precision=PREC)
    qr, qi = q[..., :width], q[..., width:]
    ct, st = tab["ct"], tab["st"]
    q2 = jnp.stack([qr * ct - qi * st, qr * st + qi * ct], axis=1)
    y = jnp.einsum("rckb,cka->rab", q2, tab["inv_a"], precision=PREC)
    return y.reshape(rows, tab["used"] * width)


def cmul(x, h, conj_h, width):
    xr, xi = x[..., :width], x[..., width:]
    hr, hi = h[..., :width], h[..., width:]
    if conj_h:
        return jnp.concatenate([xr * hr + xi * hi, xi * hr - xr * hi], axis=-1)
    return jnp.concatenate([xr * hr - xi * hi, xr * hi + xi * hr], axis=-1)


def local(
    query_pol,
    keys_pol,
    value_pol,
    filter_pol,
    skip_pol,
    query_ref,
    keys_ref,
    value_ref,
    filter_ref,
    skip_ref,
    grad_out,
):
    chan_rows, span = query_pol.shape
    group_count = filter_pol.shape[0]
    gated_pol = keys_pol.astype(jnp.float32) * value_pol.astype(jnp.float32)
    gated_ref = keys_ref.astype(jnp.float32) * value_ref.astype(jnp.float32)
    out_grad = grad_out.astype(jnp.float32)
    grad_sum = out_grad * query_pol.astype(jnp.float32)

    shards = lax.axis_size("ctx")
    own_rows = chan_rows // shards
    blocks = shards // group_count
    fields = jnp.stack([gated_pol, gated_ref, grad_sum])
    fields = fields.reshape(3, blocks, own_rows, group_count, span).transpose(1, 3, 0, 2, 4)
    fields = fields.reshape(shards, 3 * own_rows, span)
    filt = jnp.stack([filter_pol, filter_ref], axis=1)
    filt_rows = filt.shape[1]
    filt = jnp.broadcast_to(filt[None], (blocks, group_count, filt_rows, span))
    send = jnp.concatenate([fields, filt.reshape(shards, filt_rows, span)], axis=1)
    send = send.reshape(shards * (3 * own_rows + filt_rows), span)
    recv = lax.all_to_all(send, "ctx", split_axis=0, concat_axis=1, tiled=True)
    length = recv.shape[1]
    tab = dft_tables(length)
    width = tab["width"]

    spec = forward_dft(recv, tab)
    outer = spec.shape[1]
    fspec = spec[: 3 * own_rows].reshape(3, own_rows, outer, 2 * width)
    hpol = spec[3 * own_rows : 3 * own_rows + 1]
    href = spec[3 * own_rows + 1 :]
    conv_pol = cmul(fspec[0], hpol, False, width)
    conv_ref = cmul(fspec[1], href, False, width)
    corr = cmul(fspec[2], hpol, True, width)
    cross = jnp.sum(cmul(fspec[2], fspec[0], True, width), axis=0, keepdims=True)
    prods = jnp.concatenate([conv_pol, conv_ref, corr, cross], axis=0)
    back = inverse_dft(prods, tab)
    returned = lax.all_to_all(back, "ctx", split_axis=1, concat_axis=0, tiled=True)
    returned = returned.reshape(blocks, group_count, 3 * own_rows + 1, span)
    grad_filter = jnp.sum(returned[:, :, 3 * own_rows], axis=0)
    chan_size = lax.axis_size("chan")
    bit = 1
    while bit < chan_size:
        pairs = [(i, i ^ bit) for i in range(chan_size)]
        grad_filter = grad_filter + lax.ppermute(grad_filter, "chan", pairs)
        bit *= 2
    returned = returned[:, :, : 3 * own_rows].reshape(blocks, group_count, 3, own_rows, span)
    returned = returned.transpose(2, 0, 3, 1, 4).reshape(3, chan_rows, span)

    mix_pol = returned[0] + skip_pol[:, None] * gated_pol
    mix_ref = returned[1] + skip_ref[:, None] * gated_ref
    grad_mix = returned[2] + skip_pol[:, None] * grad_sum
    out_pol = (query_pol.astype(jnp.float32) * mix_pol).astype(jnp.bfloat16)
    out_ref = (query_ref.astype(jnp.float32) * mix_ref).astype(jnp.bfloat16)
    grad_query = (out_grad * mix_pol).astype(jnp.bfloat16)
    grad_keys = (grad_mix * value_pol.astype(jnp.float32)).astype(jnp.bfloat16)
    grad_value = (grad_mix * keys_pol.astype(jnp.float32)).astype(jnp.bfloat16)
    return (out_pol, out_ref, grad_query, grad_keys, grad_value, grad_filter)


def solution(mesh):
    in_specs = (
        P("chan", "ctx"),
        P("chan", "ctx"),
        P("chan", "ctx"),
        P(None, "ctx"),
        P("chan"),
        P("chan", "ctx"),
        P("chan", "ctx"),
        P("chan", "ctx"),
        P(None, "ctx"),
        P("chan"),
        P("chan", "ctx"),
    )
    out_specs = (
        P("chan", "ctx"),
        P("chan", "ctx"),
        P("chan", "ctx"),
        P("chan", "ctx"),
        P("chan", "ctx"),
        P(None, "ctx"),
    )
    return jax.shard_map(local, mesh=mesh, in_specs=in_specs, out_specs=out_specs, check_vma=False)
```

```python
import math

import jax
import jax.numpy as jnp
import numpy as np
from jax import lax
from jax.sharding import PartitionSpec as P

PREC = lax.Precision.HIGH
LANES = 128
NEAR = 4


def dft_tables(length):
    full = 2 * length
    width = LANES
    outer = full // width
    used = length // width
    a = np.arange(outer)
    b = np.arange(width)
    turn_a = 2.0 * math.pi * ((a[:, None] * a[None, :]) % outer) / outer
    turn_t = 2.0 * math.pi * ((a[:, None] * b[None, :]) % full) / full
    turn_b = 2.0 * math.pi * ((b[:, None] * b[None, :]) % width) / width
    ca, sa = np.cos(turn_a), np.sin(turn_a)
    ct, st = np.cos(turn_t), np.sin(turn_t)
    cb, sb = np.cos(turn_b), np.sin(turn_b)
    fwd_a = np.stack([ca[:, :used], -sa[:, :used]])
    fwd_b = np.block([[cb, -sb], [sb, cb]])
    inv_b = np.block([[cb, sb], [-sb, cb]])
    inv_a = np.stack([ca[:, :used], -sa[:, :used]]) / full
    f32 = lambda t: jnp.asarray(t.astype(np.float32))
    return dict(
        fwd_a=f32(fwd_a), fwd_b=f32(fwd_b), inv_b=f32(inv_b), inv_a=f32(inv_a),
        ct=f32(ct), st=f32(st), outer=outer, used=used, width=width,
    )


def forward_dft(x, tab):
    rows = x.shape[0]
    xa = x.reshape(rows, tab["used"], tab["width"])
    y = jnp.einsum("rab,cka->rckb", xa, tab["fwd_a"], precision=PREC)
    yr, yi = y[:, 0], y[:, 1]
    ct, st = tab["ct"], tab["st"]
    zr = yr * ct + yi * st
    zi = yi * ct - yr * st
    z = jnp.concatenate([zr, zi], axis=-1)
    return jnp.einsum("rkb,bm->rkm", z, tab["fwd_b"], precision=PREC)


def inverse_dft(p, tab):
    rows = p.shape[0]
    width = tab["width"]
    q = jnp.einsum("rkb,bm->rkm", p, tab["inv_b"], precision=PREC)
    qr, qi = q[..., :width], q[..., width:]
    ct, st = tab["ct"], tab["st"]
    q2 = jnp.stack([qr * ct - qi * st, qr * st + qi * ct], axis=1)
    y = jnp.einsum("rckb,cka->rab", q2, tab["inv_a"], precision=PREC)
    return y.reshape(rows, tab["used"] * width)


def cmul(x, h, conj_h, width):
    xr, xi = x[..., :width], x[..., width:]
    hr, hi = h[..., :width], h[..., width:]
    if conj_h:
        return jnp.concatenate([xr * hr + xi * hi, xi * hr - xr * hi], axis=-1)
    return jnp.concatenate([xr * hr - xi * hi, xr * hi + xi * hr], axis=-1)


def two_stage_all_to_all(block, near):
    shards = block.shape[0]
    far = shards // near
    near_groups = [[f * near + r for r in range(near)] for f in range(far)]
    far_groups = [[f * near + r for f in range(far)] for r in range(near)]
    rest = block.shape[1:]
    step = block.reshape((far, near) + rest).swapaxes(0, 1)
    step = lax.all_to_all(step, "ctx", 0, 0, axis_index_groups=near_groups, tiled=True)
    step = step.swapaxes(0, 1)
    step = lax.all_to_all(step, "ctx", 0, 0, axis_index_groups=far_groups, tiled=True)
    return step.reshape((shards,) + rest)


def local(
    query_pol,
    keys_pol,
    value_pol,
    filter_pol,
    skip_pol,
    query_ref,
    keys_ref,
    value_ref,
    filter_ref,
    skip_ref,
    grad_out,
):
    chan_rows, span = query_pol.shape
    group_count = filter_pol.shape[0]
    gated_pol = keys_pol.astype(jnp.float32) * value_pol.astype(jnp.float32)
    gated_ref = keys_ref.astype(jnp.float32) * value_ref.astype(jnp.float32)
    out_grad = grad_out.astype(jnp.float32)
    grad_sum = out_grad * query_pol.astype(jnp.float32)

    shards = lax.axis_size("ctx")
    own_rows = chan_rows // shards
    blocks = shards // group_count
    fields = jnp.stack([gated_pol, gated_ref, grad_sum])
    fields = fields.reshape(3, blocks, own_rows, group_count, span).transpose(1, 3, 0, 2, 4)
    fields = fields.reshape(shards, 3 * own_rows, span)
    filt = jnp.stack([filter_pol, filter_ref], axis=1)
    filt_rows = filt.shape[1]
    filt = jnp.broadcast_to(filt[None], (blocks, group_count, filt_rows, span))
    send = jnp.concatenate([fields, filt.reshape(shards, filt_rows, span)], axis=1)
    recv = two_stage_all_to_all(send, NEAR)
    recv = recv.transpose(1, 0, 2).reshape(3 * own_rows + filt_rows, shards * span)
    length = recv.shape[1]
    tab = dft_tables(length)
    width = tab["width"]

    spec = forward_dft(recv, tab)
    outer = spec.shape[1]
    fspec = spec[: 3 * own_rows].reshape(3, own_rows, outer, 2 * width)
    hpol = spec[3 * own_rows : 3 * own_rows + 1]
    href = spec[3 * own_rows + 1 :]
    conv_pol = cmul(fspec[0], hpol, False, width)
    conv_ref = cmul(fspec[1], href, False, width)
    corr = cmul(fspec[2], hpol, True, width)
    cross = jnp.sum(cmul(fspec[2], fspec[0], True, width), axis=0, keepdims=True)
    prods = jnp.concatenate([conv_pol, conv_ref, corr, cross], axis=0)
    back = inverse_dft(prods, tab)
    back = back.reshape(back.shape[0], shards, span).transpose(1, 0, 2)
    returned = two_stage_all_to_all(back, NEAR)
    returned = returned.reshape(blocks, group_count, 3 * own_rows + 1, span)
    grad_filter = jnp.sum(returned[:, :, 3 * own_rows], axis=0)
    chan_size = lax.axis_size("chan")
    bit = 1
    while bit < chan_size:
        pairs = [(i, i ^ bit) for i in range(chan_size)]
        grad_filter = grad_filter + lax.ppermute(grad_filter, "chan", pairs)
        bit *= 2
    returned = returned[:, :, : 3 * own_rows].reshape(blocks, group_count, 3, own_rows, span)
    returned = returned.transpose(2, 0, 3, 1, 4).reshape(3, chan_rows, span)

    mix_pol = returned[0] + skip_pol[:, None] * gated_pol
    mix_ref = returned[1] + skip_ref[:, None] * gated_ref
    grad_mix = returned[2] + skip_pol[:, None] * grad_sum
    out_pol = (query_pol.astype(jnp.float32) * mix_pol).astype(jnp.bfloat16)
    out_ref = (query_ref.astype(jnp.float32) * mix_ref).astype(jnp.bfloat16)
    grad_query = (out_grad * mix_pol).astype(jnp.bfloat16)
    grad_keys = (grad_mix * value_pol.astype(jnp.float32)).astype(jnp.bfloat16)
    grad_value = (grad_mix * keys_pol.astype(jnp.float32)).astype(jnp.bfloat16)
    return (out_pol, out_ref, grad_query, grad_keys, grad_value, grad_filter)


def solution(mesh):
    in_specs = (
        P("chan", "ctx"),
        P("chan", "ctx"),
        P("chan", "ctx"),
        P(None, "ctx"),
        P("chan"),
        P("chan", "ctx"),
        P("chan", "ctx"),
        P("chan", "ctx"),
        P(None, "ctx"),
        P("chan"),
        P("chan", "ctx"),
    )
    out_specs = (
        P("chan", "ctx"),
        P("chan", "ctx"),
        P("chan", "ctx"),
        P("chan", "ctx"),
        P("chan", "ctx"),
        P(None, "ctx"),
    )
    return jax.shard_map(local, mesh=mesh, in_specs=in_specs, out_specs=out_specs, check_vma=False)
```

```python
import math

import jax
import jax.numpy as jnp
import numpy as np
from jax import lax
from jax.sharding import PartitionSpec as P

PREC = lax.Precision.HIGH
LANES = 128


def dft_tables(length):
    full = 2 * length
    width = LANES
    outer = full // width
    used = length // width
    a = np.arange(outer)
    b = np.arange(width)
    turn_a = 2.0 * math.pi * ((a[:, None] * a[None, :]) % outer) / outer
    turn_t = 2.0 * math.pi * ((a[:, None] * b[None, :]) % full) / full
    turn_b = 2.0 * math.pi * ((b[:, None] * b[None, :]) % width) / width
    ca, sa = np.cos(turn_a), np.sin(turn_a)
    ct, st = np.cos(turn_t), np.sin(turn_t)
    cb, sb = np.cos(turn_b), np.sin(turn_b)
    fwd_a = np.stack([ca[:, :used], -sa[:, :used]])
    fwd_b = np.block([[cb, -sb], [sb, cb]])
    inv_b = np.block([[cb, sb], [-sb, cb]])
    inv_a = np.stack([ca[:, :used], -sa[:, :used]]) / full
    f32 = lambda t: jnp.asarray(t.astype(np.float32))
    return dict(
        fwd_a=f32(fwd_a), fwd_b=f32(fwd_b), inv_b=f32(inv_b), inv_a=f32(inv_a),
        ct=f32(ct), st=f32(st), outer=outer, used=used, width=width,
    )


def forward_dft(x, tab):
    rows = x.shape[0]
    xa = x.reshape(rows, tab["used"], tab["width"])
    y = jnp.einsum("rab,cka->rckb", xa, tab["fwd_a"], precision=PREC)
    yr, yi = y[:, 0], y[:, 1]
    ct, st = tab["ct"], tab["st"]
    zr = yr * ct + yi * st
    zi = yi * ct - yr * st
    z = jnp.concatenate([zr, zi], axis=-1)
    return jnp.einsum("rkb,bm->rkm", z, tab["fwd_b"], precision=PREC)


def inverse_dft(p, tab):
    rows = p.shape[0]
    width = tab["width"]
    q = jnp.einsum("rkb,bm->rkm", p, tab["inv_b"], precision=PREC)
    qr, qi = q[..., :width], q[..., width:]
    ct, st = tab["ct"], tab["st"]
    q2 = jnp.stack([qr * ct - qi * st, qr * st + qi * ct], axis=1)
    y = jnp.einsum("rckb,cka->rab", q2, tab["inv_a"], precision=PREC)
    return y.reshape(rows, tab["used"] * width)


def cmul(x, h, conj_h, width):
    xr, xi = x[..., :width], x[..., width:]
    hr, hi = h[..., :width], h[..., width:]
    if conj_h:
        return jnp.concatenate([xr * hr + xi * hi, xi * hr - xr * hi], axis=-1)
    return jnp.concatenate([xr * hr - xi * hi, xr * hi + xi * hr], axis=-1)


def local(
    query_pol,
    keys_pol,
    value_pol,
    filter_pol,
    skip_pol,
    query_ref,
    keys_ref,
    value_ref,
    filter_ref,
    skip_ref,
    grad_out,
):
    chan_rows, span = query_pol.shape
    group_count = filter_pol.shape[0]
    gated_pol = keys_pol.astype(jnp.float32) * value_pol.astype(jnp.float32)
    gated_ref = keys_ref.astype(jnp.float32) * value_ref.astype(jnp.float32)
    out_grad = grad_out.astype(jnp.float32)
    grad_sum = out_grad * query_pol.astype(jnp.float32)

    shards = lax.axis_size("ctx")
    own_rows = chan_rows // shards
    blocks = shards // group_count
    fields = jnp.stack([gated_pol, gated_ref, grad_sum])
    fields = fields.reshape(3, blocks, own_rows, group_count, span).transpose(1, 3, 0, 2, 4)
    fields = fields.reshape(shards, 3 * own_rows, span)
    filt = jnp.stack([filter_pol, filter_ref], axis=1)
    filt_rows = filt.shape[1]
    filt = jnp.broadcast_to(filt[None], (blocks, group_count, filt_rows, span))
    send = jnp.concatenate([fields, filt.reshape(shards, filt_rows, span)], axis=1)
    send = send.reshape(shards * (3 * own_rows + filt_rows), span)
    recv = lax.all_to_all(send, "ctx", split_axis=0, concat_axis=1, tiled=True)
    length = recv.shape[1]
    tab = dft_tables(length)
    width = tab["width"]

    spec = forward_dft(recv, tab)
    outer = spec.shape[1]
    fspec = spec[: 3 * own_rows].reshape(3, own_rows, outer, 2 * width)
    hpol = spec[3 * own_rows : 3 * own_rows + 1]
    href = spec[3 * own_rows + 1 :]
    conv_pol = cmul(fspec[0], hpol, False, width)
    conv_ref = cmul(fspec[1], href, False, width)
    corr = cmul(fspec[2], hpol, True, width)
    cross = jnp.sum(cmul(fspec[2], fspec[0], True, width), axis=0, keepdims=True)
    partial = inverse_dft(cross, tab)
    chan_size = lax.axis_size("chan")
    bit = 1
    while bit < chan_size:
        pairs = [(i, i ^ bit) for i in range(chan_size)]
        partial = partial + lax.ppermute(partial, "chan", pairs)
        bit *= 2
    prods = jnp.concatenate([conv_pol, conv_ref, corr], axis=0)
    back = jnp.concatenate([inverse_dft(prods, tab), partial], axis=0)
    returned = lax.all_to_all(back, "ctx", split_axis=1, concat_axis=0, tiled=True)
    returned = returned.reshape(blocks, group_count, 3 * own_rows + 1, span)
    grad_filter = jnp.sum(returned[:, :, 3 * own_rows], axis=0)
    returned = returned[:, :, : 3 * own_rows].reshape(blocks, group_count, 3, own_rows, span)
    returned = returned.transpose(2, 0, 3, 1, 4).reshape(3, chan_rows, span)

    mix_pol = returned[0] + skip_pol[:, None] * gated_pol
    mix_ref = returned[1] + skip_ref[:, None] * gated_ref
    grad_mix = returned[2] + skip_pol[:, None] * grad_sum
    out_pol = (query_pol.astype(jnp.float32) * mix_pol).astype(jnp.bfloat16)
    out_ref = (query_ref.astype(jnp.float32) * mix_ref).astype(jnp.bfloat16)
    grad_query = (out_grad * mix_pol).astype(jnp.bfloat16)
    grad_keys = (grad_mix * value_pol.astype(jnp.float32)).astype(jnp.bfloat16)
    grad_value = (grad_mix * keys_pol.astype(jnp.float32)).astype(jnp.bfloat16)
    return (out_pol, out_ref, grad_query, grad_keys, grad_value, grad_filter)


def solution(mesh):
    in_specs = (
        P("chan", "ctx"),
        P("chan", "ctx"),
        P("chan", "ctx"),
        P(None, "ctx"),
        P("chan"),
        P("chan", "ctx"),
        P("chan", "ctx"),
        P("chan", "ctx"),
        P(None, "ctx"),
        P("chan"),
        P("chan", "ctx"),
    )
    out_specs = (
        P("chan", "ctx"),
        P("chan", "ctx"),
        P("chan", "ctx"),
        P("chan", "ctx"),
        P("chan", "ctx"),
        P(None, "ctx"),
    )
    return jax.shard_map(local, mesh=mesh, in_specs=in_specs, out_specs=out_specs, check_vma=False)
```

```python
import math

import jax
import jax.numpy as jnp
import numpy as np
from jax import lax
from jax.sharding import PartitionSpec as P

PREC = lax.Precision.HIGH
LANES = 128


def dft_tables(length):
    full = 2 * length
    width = LANES
    outer = full // width
    used = length // width
    a = np.arange(outer)
    b = np.arange(width)
    turn_a = 2.0 * math.pi * ((a[:, None] * a[None, :]) % outer) / outer
    turn_t = 2.0 * math.pi * ((a[:, None] * b[None, :]) % full) / full
    turn_b = 2.0 * math.pi * ((b[:, None] * b[None, :]) % width) / width
    ca, sa = np.cos(turn_a), np.sin(turn_a)
    ct, st = np.cos(turn_t), np.sin(turn_t)
    cb, sb = np.cos(turn_b), np.sin(turn_b)
    fwd_a = np.stack([ca[:, :used], -sa[:, :used]])
    fwd_b = np.block([[cb, -sb], [sb, cb]])
    inv_b = np.block([[cb, sb], [-sb, cb]])
    inv_a = np.stack([ca[:, :used], -sa[:, :used]]) / full
    f32 = lambda t: jnp.asarray(t.astype(np.float32))
    return dict(
        fwd_a=f32(fwd_a), fwd_b=f32(fwd_b), inv_b=f32(inv_b), inv_a=f32(inv_a),
        ct=f32(ct), st=f32(st), outer=outer, used=used, width=width,
    )


def forward_dft(x, tab):
    rows = x.shape[0]
    xa = x.reshape(rows, tab["used"], tab["width"])
    y = jnp.einsum("rab,cka->rckb", xa, tab["fwd_a"], precision=PREC)
    yr, yi = y[:, 0], y[:, 1]
    ct, st = tab["ct"], tab["st"]
    zr = yr * ct + yi * st
    zi = yi * ct - yr * st
    z = jnp.concatenate([zr, zi], axis=-1)
    return jnp.einsum("rkb,bm->rkm", z, tab["fwd_b"], precision=PREC)


def inverse_dft(p, tab):
    rows = p.shape[0]
    width = tab["width"]
    q = jnp.einsum("rkb,bm->rkm", p, tab["inv_b"], precision=PREC)
    qr, qi = q[..., :width], q[..., width:]
    ct, st = tab["ct"], tab["st"]
    q2 = jnp.stack([qr * ct - qi * st, qr * st + qi * ct], axis=1)
    y = jnp.einsum("rckb,cka->rab", q2, tab["inv_a"], precision=PREC)
    return y.reshape(rows, tab["used"] * width)


def cmul(x, h, conj_h, width):
    xr, xi = x[..., :width], x[..., width:]
    hr, hi = h[..., :width], h[..., width:]
    if conj_h:
        return jnp.concatenate([xr * hr + xi * hi, xi * hr - xr * hi], axis=-1)
    return jnp.concatenate([xr * hr - xi * hi, xr * hi + xi * hr], axis=-1)


def local(
    query_pol,
    keys_pol,
    value_pol,
    filter_pol,
    skip_pol,
    query_ref,
    keys_ref,
    value_ref,
    filter_ref,
    skip_ref,
    grad_out,
):
    chan_rows, span = query_pol.shape
    group_count = filter_pol.shape[0]
    gated_pol = keys_pol.astype(jnp.float32) * value_pol.astype(jnp.float32)
    gated_ref = keys_ref.astype(jnp.float32) * value_ref.astype(jnp.float32)
    out_grad = grad_out.astype(jnp.float32)
    grad_sum = out_grad * query_pol.astype(jnp.float32)

    shards = lax.axis_size("ctx")
    own_rows = chan_rows // shards
    blocks = shards // group_count
    fields = jnp.stack([gated_pol, gated_ref, grad_sum])
    fields = fields.reshape(3, blocks, own_rows, group_count, span).transpose(1, 3, 0, 2, 4)
    fields = fields.reshape(shards, 3 * own_rows, span)
    filt = jnp.stack([filter_pol, filter_ref], axis=1)
    filt_rows = filt.shape[1]
    filt = jnp.broadcast_to(filt[None], (blocks, group_count, filt_rows, span))
    send = jnp.concatenate([fields, filt.reshape(shards, filt_rows, span)], axis=1)
    rows_in = 3 * own_rows + filt_rows
    send = send.reshape(shards, 1, rows_in * span)
    recv = lax.all_to_all(send, "ctx", split_axis=0, concat_axis=0, tiled=True)
    recv = recv.reshape(shards, rows_in, span).transpose(1, 0, 2).reshape(rows_in, shards * span)
    length = recv.shape[1]
    tab = dft_tables(length)
    width = tab["width"]

    spec = forward_dft(recv, tab)
    outer = spec.shape[1]
    fspec = spec[: 3 * own_rows].reshape(3, own_rows, outer, 2 * width)
    hpol = spec[3 * own_rows : 3 * own_rows + 1]
    href = spec[3 * own_rows + 1 :]
    conv_pol = cmul(fspec[0], hpol, False, width)
    conv_ref = cmul(fspec[1], href, False, width)
    corr = cmul(fspec[2], hpol, True, width)
    cross = jnp.sum(cmul(fspec[2], fspec[0], True, width), axis=0, keepdims=True)
    partial = inverse_dft(cross, tab)
    chan_size = lax.axis_size("chan")
    bit = 1
    while bit < chan_size:
        pairs = [(i, i ^ bit) for i in range(chan_size)]
        partial = partial + lax.ppermute(partial, "chan", pairs)
        bit *= 2
    prods = jnp.concatenate([conv_pol, conv_ref, corr], axis=0)
    back = jnp.concatenate([inverse_dft(prods, tab), partial], axis=0)
    rows_out = back.shape[0]
    back = back.reshape(rows_out, shards, span).transpose(1, 0, 2).reshape(shards, 1, rows_out * span)
    returned = lax.all_to_all(back, "ctx", split_axis=0, concat_axis=0, tiled=True)
    returned = returned.reshape(blocks, group_count, 3 * own_rows + 1, span)
    grad_filter = jnp.sum(returned[:, :, 3 * own_rows], axis=0)
    returned = returned[:, :, : 3 * own_rows].reshape(blocks, group_count, 3, own_rows, span)
    returned = returned.transpose(2, 0, 3, 1, 4).reshape(3, chan_rows, span)

    mix_pol = returned[0] + skip_pol[:, None] * gated_pol
    mix_ref = returned[1] + skip_ref[:, None] * gated_ref
    grad_mix = returned[2] + skip_pol[:, None] * grad_sum
    out_pol = (query_pol.astype(jnp.float32) * mix_pol).astype(jnp.bfloat16)
    out_ref = (query_ref.astype(jnp.float32) * mix_ref).astype(jnp.bfloat16)
    grad_query = (out_grad * mix_pol).astype(jnp.bfloat16)
    grad_keys = (grad_mix * value_pol.astype(jnp.float32)).astype(jnp.bfloat16)
    grad_value = (grad_mix * keys_pol.astype(jnp.float32)).astype(jnp.bfloat16)
    return (out_pol, out_ref, grad_query, grad_keys, grad_value, grad_filter)


def solution(mesh):
    in_specs = (
        P("chan", "ctx"),
        P("chan", "ctx"),
        P("chan", "ctx"),
        P(None, "ctx"),
        P("chan"),
        P("chan", "ctx"),
        P("chan", "ctx"),
        P("chan", "ctx"),
        P(None, "ctx"),
        P("chan"),
        P("chan", "ctx"),
    )
    out_specs = (
        P("chan", "ctx"),
        P("chan", "ctx"),
        P("chan", "ctx"),
        P("chan", "ctx"),
        P("chan", "ctx"),
        P(None, "ctx"),
    )
    return jax.shard_map(local, mesh=mesh, in_specs=in_specs, out_specs=out_specs, check_vma=False)
```

```python
import math

import jax
import jax.numpy as jnp
import numpy as np
from jax import lax
from jax.sharding import PartitionSpec as P

PREC = lax.Precision.HIGH
LANES = 128


def dft_tables(length):
    full = 2 * length
    width = LANES
    outer = full // width
    used = length // width
    a = np.arange(outer)
    b = np.arange(width)
    turn_a = 2.0 * math.pi * ((a[:, None] * a[None, :]) % outer) / outer
    turn_t = 2.0 * math.pi * ((a[:, None] * b[None, :]) % full) / full
    turn_b = 2.0 * math.pi * ((b[:, None] * b[None, :]) % width) / width
    ca, sa = np.cos(turn_a), np.sin(turn_a)
    ct, st = np.cos(turn_t), np.sin(turn_t)
    cb, sb = np.cos(turn_b), np.sin(turn_b)
    fwd_a = np.stack([ca[:, :used], -sa[:, :used]])
    fwd_b = np.block([[cb, -sb], [sb, cb]])
    inv_b = np.block([[cb, sb], [-sb, cb]])
    inv_a = np.stack([ca[:, :used], -sa[:, :used]]) / full
    f32 = lambda t: jnp.asarray(t.astype(np.float32))
    return dict(
        fwd_a=f32(fwd_a), fwd_b=f32(fwd_b), inv_b=f32(inv_b), inv_a=f32(inv_a),
        ct=f32(ct), st=f32(st), outer=outer, used=used, width=width,
    )


def forward_dft(x, tab):
    rows = x.shape[0]
    xa = x.reshape(rows, tab["used"], tab["width"])
    y = jnp.einsum("rab,cka->rckb", xa, tab["fwd_a"], precision=PREC)
    yr, yi = y[:, 0], y[:, 1]
    ct, st = tab["ct"], tab["st"]
    zr = yr * ct + yi * st
    zi = yi * ct - yr * st
    z = jnp.concatenate([zr, zi], axis=-1)
    return jnp.einsum("rkb,bm->rkm", z, tab["fwd_b"], precision=PREC)


def inverse_dft(p, tab):
    rows = p.shape[0]
    width = tab["width"]
    q = jnp.einsum("rkb,bm->rkm", p, tab["inv_b"], precision=PREC)
    qr, qi = q[..., :width], q[..., width:]
    ct, st = tab["ct"], tab["st"]
    q2 = jnp.stack([qr * ct - qi * st, qr * st + qi * ct], axis=1)
    y = jnp.einsum("rckb,cka->rab", q2, tab["inv_a"], precision=PREC)
    return y.reshape(rows, tab["used"] * width)


def cmul(x, h, conj_h, width):
    xr, xi = x[..., :width], x[..., width:]
    hr, hi = h[..., :width], h[..., width:]
    if conj_h:
        return jnp.concatenate([xr * hr + xi * hi, xi * hr - xr * hi], axis=-1)
    return jnp.concatenate([xr * hr - xi * hi, xr * hi + xi * hr], axis=-1)


def local(
    query_pol,
    keys_pol,
    value_pol,
    filter_pol,
    skip_pol,
    query_ref,
    keys_ref,
    value_ref,
    filter_ref,
    skip_ref,
    grad_out,
):
    chan_rows, span = query_pol.shape
    group_count = filter_pol.shape[0]
    gated_pol = keys_pol.astype(jnp.float32) * value_pol.astype(jnp.float32)
    gated_ref = keys_ref.astype(jnp.float32) * value_ref.astype(jnp.float32)
    out_grad = grad_out.astype(jnp.float32)
    grad_sum = out_grad * query_pol.astype(jnp.float32)

    shards = lax.axis_size("ctx")
    own_rows = chan_rows // shards
    blocks = shards // group_count
    fields = jnp.stack([gated_pol, gated_ref, grad_sum])
    fields = fields.reshape(3, blocks, own_rows, group_count, span).transpose(1, 3, 0, 2, 4)
    fields = fields.reshape(shards, 3 * own_rows, span)
    filt = jnp.stack([filter_pol, filter_ref], axis=1)
    filt_rows = filt.shape[1]
    filt = jnp.broadcast_to(filt[None], (blocks, group_count, filt_rows, span))
    send = jnp.concatenate([fields, filt.reshape(shards, filt_rows, span)], axis=1)
    rows_in = 3 * own_rows + filt_rows
    send = send.reshape(shards, 1, rows_in * span)
    recv = lax.all_to_all(send, "ctx", split_axis=0, concat_axis=0, tiled=True)
    recv = recv.reshape(shards, rows_in, span).transpose(1, 0, 2).reshape(rows_in, shards * span)
    length = recv.shape[1]
    tab = dft_tables(length)
    width = tab["width"]

    spec = forward_dft(recv, tab)
    outer = spec.shape[1]
    fspec = spec[: 3 * own_rows].reshape(3, own_rows, outer, 2 * width)
    hpol = spec[3 * own_rows : 3 * own_rows + 1]
    href = spec[3 * own_rows + 1 :]
    conv_pol = cmul(fspec[0], hpol, False, width)
    conv_ref = cmul(fspec[1], href, False, width)
    corr = cmul(fspec[2], hpol, True, width)
    cross = jnp.sum(cmul(fspec[2], fspec[0], True, width), axis=0, keepdims=True)
    partial = inverse_dft(cross, tab)
    chan_size = lax.axis_size("chan")
    shifted = [partial] + [
        lax.ppermute(partial, "chan", [(i, (i + k) % chan_size) for i in range(chan_size)])
        for k in range(1, chan_size)
    ]
    shifted = jnp.stack(shifted)
    me = lax.axis_index("chan")
    order = (me - jnp.arange(chan_size, dtype=jnp.int32)) % chan_size
    partial = jnp.sum(jnp.take(shifted, order, axis=0), axis=0)
    prods = jnp.concatenate([conv_pol, conv_ref, corr], axis=0)
    back = jnp.concatenate([inverse_dft(prods, tab), partial], axis=0)
    rows_out = back.shape[0]
    back = back.reshape(rows_out, shards, span).transpose(1, 0, 2).reshape(shards, 1, rows_out * span)
    returned = lax.all_to_all(back, "ctx", split_axis=0, concat_axis=0, tiled=True)
    returned = returned.reshape(blocks, group_count, 3 * own_rows + 1, span)
    grad_filter = jnp.sum(returned[:, :, 3 * own_rows], axis=0)
    returned = returned[:, :, : 3 * own_rows].reshape(blocks, group_count, 3, own_rows, span)
    returned = returned.transpose(2, 0, 3, 1, 4).reshape(3, chan_rows, span)

    mix_pol = returned[0] + skip_pol[:, None] * gated_pol
    mix_ref = returned[1] + skip_ref[:, None] * gated_ref
    grad_mix = returned[2] + skip_pol[:, None] * grad_sum
    out_pol = (query_pol.astype(jnp.float32) * mix_pol).astype(jnp.bfloat16)
    out_ref = (query_ref.astype(jnp.float32) * mix_ref).astype(jnp.bfloat16)
    grad_query = (out_grad * mix_pol).astype(jnp.bfloat16)
    grad_keys = (grad_mix * value_pol.astype(jnp.float32)).astype(jnp.bfloat16)
    grad_value = (grad_mix * keys_pol.astype(jnp.float32)).astype(jnp.bfloat16)
    return (out_pol, out_ref, grad_query, grad_keys, grad_value, grad_filter)


def solution(mesh):
    in_specs = (
        P("chan", "ctx"),
        P("chan", "ctx"),
        P("chan", "ctx"),
        P(None, "ctx"),
        P("chan"),
        P("chan", "ctx"),
        P("chan", "ctx"),
        P("chan", "ctx"),
        P(None, "ctx"),
        P("chan"),
        P("chan", "ctx"),
    )
    out_specs = (
        P("chan", "ctx"),
        P("chan", "ctx"),
        P("chan", "ctx"),
        P("chan", "ctx"),
        P("chan", "ctx"),
        P(None, "ctx"),
    )
    return jax.shard_map(local, mesh=mesh, in_specs=in_specs, out_specs=out_specs, check_vma=False)
```
